128 devices in a mesh: seq: 4 (over x), ctx: 32 (over z, y, core).
Axes of the slice: x: 4, y: 4, z: 4, core: 2. Of those that a mesh axis runs over, the one named last changes fastest.
Arguments:
- delta_query: bfloat16 [4, 4096, 2048], P('seq', 'ctx'), may hold values from -6 to 6
- delta_key: bfloat16 [4, 4096, 2048], P('seq', 'ctx'), may hold values from -6 to 6
- delta_value: bfloat16 [4, 4096, 4096], P('seq', 'ctx'), may hold values from -6 to 6
- delta_gate: bfloat16 [4, 4096, 4096], P('seq', 'ctx'), may hold values from -6 to 6
- delta_beta: float32 [4, 32, 4096], P('seq', None, 'ctx'), may hold values from 0 to 1
- delta_decay: float32 [4, 32, 4096], P('seq', None, 'ctx'), may hold values from -2 to 0
- norm_gain: float32 [128], replicated, may hold values from 0.5 to 1.5
- attention_query: bfloat16 [4, 4096, 4096], P('seq', 'ctx'), may hold values from -4 to 4
- attention_key_value: bfloat16 [4, 4096, 1024], P('seq', 'ctx'), may hold values from -4 to 4
- attention_gate: bfloat16 [4, 4096, 4096], P('seq', 'ctx'), may hold values from -6 to 6
- moe_input: bfloat16 [4, 4096, 2048], P('seq', 'ctx'), may hold values from -6 to 6
- routes: int32 [4, 4096, 10], P('seq', 'ctx'), may hold values from 0 to 127, all different within a row; in each aligned block of 128 rows (0 to 127, 128 to 255, ..., all dimensions but the last counted through in order) at most 16 rows name the same one
- drop_mask: int32 [4, 4096, 10], P('seq', 'ctx'), may hold values 0 or 1
- route_weights: float32 [4, 4096, 10], P('seq', 'ctx'), may hold values from 0.05 to 0.5
- w_gate: bfloat16 [128, 2048, 512], P(('seq', 'ctx')), may hold values from -0.125 to 0.125
- w_up: bfloat16 [128, 2048, 512], P(('seq', 'ctx')), may hold values from -0.125 to 0.125
- w_down: bfloat16 [128, 512, 2048], P(('seq', 'ctx')), may hold values from -0.25 to 0.25
Outputs:
- delta_out: bfloat16 [4, 4096, 4096], P('seq', 'ctx')
- attn_out: bfloat16 [4, 4096, 4096], P('seq', 'ctx')
- moe_out: bfloat16 [4, 4096, 2048], P('seq', 'ctx')
The draws below stay inside these ranges and needn't reach their ends.
Inputs may be any that keep to these rules, and one draw needn't show every extreme that they name: `routes`: within the rows of one device (aligned blocks of 128 positions), each token names 10 different experts and no expert is named more than 16 times; in some block some expert is named exactly 16 times. `drop_mask`: 1 keeps the chosen expert, 0 drops it.
All inputs are finite; a program needn't handle non-finite values. No bound on the sum of `drop_mask` on one device may be relied on, other than what follows from the above.
Results may differ from the reference program's by a relative error of at most 0.011.
Values may be sent and summed in bfloat16 or wider, within the bound.
No kernel may reach another device: no remote copies, remote signals or barrier semaphores. Data moves between devices by JAX's collectives and lax.ppermute only.
A program may use at most 384 MiB of HBM per device.

```python
import math
import jax
import jax.numpy as jnp
import numpy as np
from jax import lax

D = 2048
HV = 32
HKD = 16
DK = 128
DV = 128
QUERY_HEADS = 16
KEY_VALUE_HEADS = 2
HEAD_WIDTH = 256
FFE = 512
TOP = 10
SPAN = 64
LOCAL_TOKENS = 128
SEQUENCE_COUNT = 4
SEQUENCE_LENGTH = 4096
EXPERTS = 128
CAP = 16


def head_classes(key):
    share = 0.5
    return jax.random.uniform(key, (SEQUENCE_COUNT, HV, 1)) < share


def log_uniform(key, shape, lower, upper):
    return jnp.exp(jax.random.uniform(key, shape, jnp.float32, math.log(lower), math.log(upper)))


def draw_delta_decay(key, part):
    slow = head_classes(jax.random.fold_in(key, 3))
    slow_rate = log_uniform(jax.random.fold_in(key, 31), (SEQUENCE_COUNT, HV, 1), 0.05, 0.3) / SEQUENCE_LENGTH
    fast_rate = log_uniform(jax.random.fold_in(key, 32), (SEQUENCE_COUNT, HV, 1), 1.0 / 50.0, 1.0 / 30.0)
    head_rate = jnp.where(slow, slow_rate, fast_rate)
    block_list = SEQUENCE_LENGTH // LOCAL_TOKENS
    device_factor = log_uniform(jax.random.fold_in(key, 33), (SEQUENCE_COUNT, HV, block_list, 1), 0.5, 2.0)
    token_factor = jax.random.uniform(jax.random.fold_in(key, 34), (SEQUENCE_COUNT, HV, block_list, LOCAL_TOKENS), jnp.float32, 0.5, 1.5)
    rate_values = (head_rate[:, :, :, None] * device_factor * token_factor).reshape(SEQUENCE_COUNT, HV, SEQUENCE_LENGTH)
    surge_position = jax.random.randint(jax.random.fold_in(key, 35), (SEQUENCE_COUNT, 3), 0, SEQUENCE_LENGTH)
    surge_depth = jax.random.uniform(jax.random.fold_in(key, 36), (SEQUENCE_COUNT, 3), jnp.float32, 0.2, 0.35)
    place_list = jnp.arange(SEQUENCE_LENGTH, dtype=jnp.int32)
    surge_list = jnp.sum(jnp.where(place_list[None, None, :] == surge_position[:, :, None], jnp.log(1.0 - surge_depth)[:, :, None], 0.0), axis=1)
    return (surge_list[:, None, :] - rate_values).astype(jnp.float32)


def draw_delta_beta(key, part):
    slow = head_classes(jax.random.fold_in(key, 3))
    slow_beta = log_uniform(jax.random.fold_in(key, 41), (SEQUENCE_COUNT, HV, SEQUENCE_LENGTH), 0.003, 0.03)
    fast_beta = jax.random.uniform(jax.random.fold_in(key, 42), (SEQUENCE_COUNT, HV, SEQUENCE_LENGTH), jnp.float32, 0.1, 0.9)
    return jnp.where(slow, slow_beta, fast_beta).astype(jnp.float32)


def draw_attention_query(key, part):
    value_rows = jnp.clip(jax.random.normal(jax.random.fold_in(key, 11), (SEQUENCE_COUNT, SEQUENCE_LENGTH, QUERY_HEADS * HEAD_WIDTH)), -4.0, 4.0)
    return value_rows.astype(jnp.bfloat16)


def draw_attention_key_value(key, part):
    value_rows = jnp.clip(jax.random.normal(jax.random.fold_in(key, 12), (SEQUENCE_COUNT, SEQUENCE_LENGTH, 2 * KEY_VALUE_HEADS * HEAD_WIDTH)), -4.0, 4.0)
    return value_rows.astype(jnp.bfloat16)


def set_ends(values, own_key, least, top_value):
    longest = values.shape.index(max(values.shape))
    spots = []
    for shift in (0, 1):
        where = [jax.random.randint(jax.random.fold_in(own_key, axis), (), 0, length) for axis, length in enumerate(values.shape)]
        where[longest] = (where[longest] + shift) % values.shape[longest]
        spots.append(tuple(where))
    return values.at[spots[0]].set(least).at[spots[1]].set(top_value)


def block_scale(stream_key, extent, cuts, low, top_value):
    def one(dim, parts):
        steps = jax.random.uniform(jax.random.fold_in(jax.random.fold_in(stream_key, 6), dim), (parts,), jnp.float32, low / len(cuts), top_value / len(cuts))
        return jnp.repeat(jnp.exp(steps), extent[dim] // parts).reshape((-1,) + (1,) * (len(extent) - dim - 1))

    gain = one(*cuts[0])
    for cut in cuts[1:]:
        gain = gain * one(*cut)
    return gain


def routed_block(key, own, number, rows, number_of, top, bound, skew):
    ranking = jax.random.permutation(key, number_of)
    heavy_load, common = shares(number_of, rows * top, bound, skew, True), shares(number_of, rows * top, bound, skew, False)
    places = jnp.arange(number_of)

    def named(lengths, offset_by):
        used = int((lengths > 0).sum())
        fixed = max(1, used // 4)
        moved = fixed + (places - fixed + offset_by * (used - fixed)) % max(1, number_of - fixed)
        return jnp.zeros((number_of,), jnp.int32).at[ranking[jnp.where(places < fixed, places, moved)]].set(jnp.asarray(lengths, jnp.int32))

    lengths = jnp.where(number % 4 == 0, named(heavy_load, number // 4), named(common, number - number // 4 - 1))
    mixed = jax.random.permutation(jax.random.fold_in(own, 3), number_of)
    giver, receiver = mixed[0:number_of // 2 * 2:2], mixed[1:number_of // 2 * 2:2]
    margin = jnp.minimum(lengths[giver] - 1, bound - lengths[receiver]) // 2
    margin = jnp.where((giver == ranking[0]) | (receiver == ranking[0]) | (lengths[receiver] == 0), 0, jnp.maximum(margin, 0))
    moved = jax.random.randint(jax.random.fold_in(own, 4), (number_of // 2,), 0, 1 << 20) % (margin + 1)
    lengths = lengths.at[giver].add(-moved).at[receiver].add(moved)
    items = jnp.searchsorted(jnp.cumsum(lengths), jnp.arange(rows * top), side="right").astype(jnp.int32)
    grid = items.reshape(top, rows).T
    grid = grid[jax.random.permutation(jax.random.fold_in(own, 1), rows)]
    offset_by = jax.random.randint(jax.random.fold_in(own, 2), (rows, 1), 0, top)
    return jnp.take_along_axis(grid, (jnp.arange(top)[None, :] + offset_by) % top, axis=1)


def shares(number_of, total, limit, skew, full):
    weights = [(1 << 20) // math.isqrt(grade ** skew) + 1 for grade in range(1, number_of + 1)]
    largest = limit if full else min(limit, max(-(-total // number_of), total * weights[0] // sum(weights)))
    least = 1 if total - largest >= number_of - 1 else 0
    counts, rest = [largest] + [least] * (number_of - 1), total - largest - least * (number_of - 1)
    while rest > 0:
        candidates = [i for i in range(1, number_of) if counts[i] < largest] or [i for i in range(1, number_of) if counts[i] < limit]
        pool, remaining = sum([weights[i] for i in candidates]), rest
        for i in candidates:
            more = min(limit - counts[i], max(1, remaining * weights[i] // pool), rest)
            counts[i] = counts[i] + more
            rest = rest - more
    return np.array(counts)


def gaussian(stream_key, shape, scale, reach, shards=(), kind=jnp.bfloat16):
    values = scale * jax.random.normal(stream_key, shape, jnp.float32)
    if shards:
        values = values * block_scale(stream_key, shape, shards, -0.22, 0.18)
    return jnp.clip(values, -reach, reach).astype(kind)


def setup_inputs(seed: int = 0) -> dict:
    key_list = jax.random.split(jax.random.key(seed), 18)
    delta_query = gaussian(key_list[0], (SEQUENCE_COUNT, SEQUENCE_LENGTH, HKD * DK), 1.0, 6.0, ((0, 4), (1, 32)))
    delta_key = gaussian(key_list[1], (SEQUENCE_COUNT, SEQUENCE_LENGTH, HKD * DK), 1.0, 6.0, ((0, 4), (1, 32)))
    delta_value = gaussian(key_list[2], (SEQUENCE_COUNT, SEQUENCE_LENGTH, HV * DV), 1.0, 6.0, ((0, 4), (1, 32)))
    delta_gate = gaussian(key_list[3], (SEQUENCE_COUNT, SEQUENCE_LENGTH, HV * DV), 1.0, 6.0, ((0, 4), (1, 32)))
    delta_beta = draw_delta_beta(jax.random.fold_in(key_list[17], 71), 0)
    delta_decay = draw_delta_decay(jax.random.fold_in(key_list[17], 71), 0)
    norm_gain = jnp.clip(1.0 + 0.1 * jax.random.normal(key_list[6], (DV,), jnp.float32), 0.5, 1.5)
    attention_query = draw_attention_query(jax.random.fold_in(key_list[17], 71), 0)
    attention_key_value = draw_attention_key_value(jax.random.fold_in(key_list[17], 71), 0)
    attention_gate = gaussian(key_list[9], (SEQUENCE_COUNT, SEQUENCE_LENGTH, QUERY_HEADS * HEAD_WIDTH), 1.0, 6.0, ((0, 4), (1, 32)))
    moe_input = gaussian(key_list[10], (SEQUENCE_COUNT, SEQUENCE_LENGTH, D), 1.0, 6.0, ((0, 4), (1, 32)))
    routes_keys = jax.random.split(jax.random.fold_in(key_list[11], 1), SEQUENCE_COUNT * SEQUENCE_LENGTH // LOCAL_TOKENS)
    routes_turns = jax.random.permutation(jax.random.fold_in(key_list[11], 3), SEQUENCE_COUNT * SEQUENCE_LENGTH // LOCAL_TOKENS)
    routes = jax.vmap(lambda own, number: routed_block(jax.random.fold_in(key_list[11], 2), own, number, LOCAL_TOKENS, EXPERTS, TOP, CAP, 1))(routes_keys, routes_turns).reshape((SEQUENCE_COUNT, SEQUENCE_LENGTH, TOP))
    drop_mask = set_ends((jax.random.randint(key_list[12], (SEQUENCE_COUNT, SEQUENCE_LENGTH, TOP), 0, 4) < 3).astype(jnp.int32), jax.random.fold_in(key_list[12], 1), 0, 1)
    route_weights = jnp.clip(jnp.exp(math.log(0.5) - 2.3025851 * jax.random.uniform(key_list[13], (SEQUENCE_COUNT, SEQUENCE_LENGTH, TOP), jnp.float32) ** block_scale(key_list[13], (SEQUENCE_COUNT, SEQUENCE_LENGTH, TOP), ((0, 4), (1, 32)), -0.2, 0.2)), 0.05, 0.5)
    w_gate = gaussian(key_list[14], (EXPERTS, D, FFE), D ** -0.5, 0.125, ((0, 128),))
    w_up = gaussian(key_list[15], (EXPERTS, D, FFE), D ** -0.5, 0.125, ((0, 128),))
    w_down = gaussian(key_list[16], (EXPERTS, FFE, D), FFE ** -0.5, 0.25, ((0, 128),))
    return {"delta_query": delta_query, "delta_key": delta_key, "delta_value": delta_value, "delta_gate": delta_gate, "delta_beta": delta_beta, "delta_decay": delta_decay, "norm_gain": norm_gain, "attention_query": attention_query, "attention_key_value": attention_key_value, "attention_gate": attention_gate, "moe_input": moe_input, "routes": routes, "drop_mask": drop_mask, "route_weights": route_weights, "w_gate": w_gate, "w_up": w_up, "w_down": w_down}


precise = lax.Precision.HIGHEST

def unit_rows(matrix):
    return matrix / jnp.sqrt(lax.optimization_barrier(jnp.sum(matrix * matrix, axis=-1, keepdims=True)) + 1e-06)

def span_terms(query_rows, keys, value_rows, beta, decay):
    size = decay.shape[-1]
    key_dim = keys.shape[-1]
    value_dim = value_rows.shape[-1]
    cumulative = jnp.cumsum(decay, axis=-1)
    place_list = jnp.arange(size)
    lower = place_list[:, None] >= place_list[None, :]
    strict = place_list[:, None] > place_list[None, :]
    spread = cumulative[..., :, None] - cumulative[..., None, :]
    decay_ratio = jnp.exp(jnp.where(lower, spread, -1e+30))
    key_key = jnp.einsum('...ik,...jk->...ij', keys, keys, precision=precise)
    query_key = jnp.einsum('...ik,...jk->...ij', query_rows, keys, precision=precise)
    system = jnp.eye(size, dtype=jnp.float32) + jnp.where(strict, beta[..., :, None] * decay_ratio * key_key, 0.0)
    retained = jnp.exp(cumulative)
    right_side = jnp.concatenate([beta[..., None] * value_rows, (beta * retained)[..., None] * keys], axis=-1)
    solved = jax.scipy.linalg.solve_triangular(system, right_side, lower=True, unit_diagonal=True)
    new_values = solved[..., :value_dim]
    new_keys = solved[..., value_dim:]
    mixing = decay_ratio * query_key
    query_eff = retained[..., None] * query_rows - jnp.einsum('...ij,...jk->...ik', mixing, new_keys, precision=precise)
    direct = jnp.einsum('...ij,...jv->...iv', mixing, new_values, precision=precise)
    tail_keys = jnp.exp(cumulative[..., -1:] - cumulative)[..., None] * keys
    carry_a = retained[..., -1:, None] * jnp.eye(key_dim, dtype=jnp.float32) - jnp.einsum('...ck,...cl->...kl', new_keys, tail_keys, precision=precise)
    carry_b = jnp.einsum('...cv,...cl->...vl', new_values, tail_keys, precision=precise)
    return (query_eff, direct, carry_a, carry_b)

def gated_norm(outputs, delta_gate, norm_gain):
    scale = lax.rsqrt(lax.optimization_barrier(jnp.mean(outputs * outputs, axis=-1, keepdims=True)) + 1e-06)
    gate_vals = delta_gate.astype(jnp.float32).reshape(outputs.shape)
    normed = outputs * scale * norm_gain * jax.nn.silu(gate_vals)
    return normed.astype(jnp.bfloat16).reshape(delta_gate.shape)

def delta_layer(delta_query, delta_key, delta_value, delta_gate, delta_beta, delta_decay, norm_gain):
    head_repeat = HV // HKD
    n_spans = SEQUENCE_LENGTH // SPAN
    query_rows = unit_rows(delta_query.astype(jnp.float32).reshape(SEQUENCE_COUNT, SEQUENCE_LENGTH, HKD, DK)) * (1.0 / math.sqrt(DK))
    query_rows = jnp.repeat(query_rows, head_repeat, axis=2)
    keys = jnp.repeat(unit_rows(delta_key.astype(jnp.float32).reshape(SEQUENCE_COUNT, SEQUENCE_LENGTH, HKD, DK)), head_repeat, axis=2)
    value_rows = delta_value.astype(jnp.float32).reshape(SEQUENCE_COUNT, SEQUENCE_LENGTH, HV, DV)

    def to_spans(array):
        return array.reshape(SEQUENCE_COUNT, n_spans, SPAN, HV, array.shape[-1]).transpose(1, 0, 3, 2, 4)

    def gate_spans(array):
        return array.reshape(SEQUENCE_COUNT, HV, n_spans, SPAN).transpose(2, 0, 1, 3)

    def advance(state, pieces):
        query_eff, direct, carry_a, carry_b = span_terms(*pieces)
        output = jnp.einsum('shck,shvk->shcv', query_eff, state, precision=precise) + direct
        state = jnp.einsum('shvk,shkl->shvl', state, carry_a, precision=precise) + carry_b
        return (state, output)
    start = jnp.zeros((SEQUENCE_COUNT, HV, DV, DK), jnp.float32)
    pieces = (to_spans(query_rows), to_spans(keys), to_spans(value_rows), gate_spans(delta_beta), gate_spans(delta_decay))
    final_state, outputs = lax.scan(advance, start, pieces)
    outputs = outputs.transpose(1, 0, 3, 2, 4).reshape(SEQUENCE_COUNT, SEQUENCE_LENGTH, HV, DV)
    return gated_norm(outputs, delta_gate, norm_gain)

def attention_layer(attention_query, attention_key_value, attention_gate):
    block_list = SEQUENCE_LENGTH // LOCAL_TOKENS
    head_groups = QUERY_HEADS // KEY_VALUE_HEADS
    query_rows = attention_query.reshape(SEQUENCE_COUNT, block_list, LOCAL_TOKENS, KEY_VALUE_HEADS, head_groups, HEAD_WIDTH)
    key_value = attention_key_value.reshape(SEQUENCE_COUNT, block_list, LOCAL_TOKENS, 2, KEY_VALUE_HEADS, HEAD_WIDTH)
    previous = jnp.concatenate([jnp.zeros_like(key_value[:, :1]), key_value[:, :-1]], axis=1)
    window = jnp.concatenate([previous, key_value], axis=2)
    gate_values = attention_gate.reshape(SEQUENCE_COUNT, block_list, LOCAL_TOKENS, KEY_VALUE_HEADS, head_groups, HEAD_WIDTH)
    starts = jnp.arange(block_list, dtype=jnp.int32) * LOCAL_TOKENS

    def one_block(pieces):
        query_block, window_block, gate_block, base = pieces
        scores = jnp.einsum('stkgd,sukd->skgtu', query_block.astype(jnp.float32), window_block[:, :, 0].astype(jnp.float32), precision=precise) * (1.0 / math.sqrt(HEAD_WIDTH))
        query_pos = base + jnp.arange(LOCAL_TOKENS, dtype=jnp.int32)
        key_pos = base - LOCAL_TOKENS + jnp.arange(2 * LOCAL_TOKENS, dtype=jnp.int32)
        visible = (key_pos[None, :] <= query_pos[:, None]) & (key_pos[None, :] > query_pos[:, None] - LOCAL_TOKENS) & (key_pos[None, :] >= 0)
        scores = jnp.where(visible, scores, -jnp.inf)
        row_max = lax.optimization_barrier(jnp.max(scores, axis=-1, keepdims=True))
        lifted = jnp.exp(scores - row_max)
        probs = (lifted / lax.optimization_barrier(jnp.sum(lifted, axis=-1, keepdims=True))).astype(jnp.bfloat16)
        mixed = jnp.einsum('skgtu,sukd->stkgd', probs.astype(jnp.float32), window_block[:, :, 1].astype(jnp.float32), precision=precise)
        gated = mixed * jax.nn.sigmoid(gate_block.astype(jnp.float32))
        return gated.astype(jnp.bfloat16).reshape(SEQUENCE_COUNT, LOCAL_TOKENS, QUERY_HEADS * HEAD_WIDTH)
    outputs = lax.map(one_block, (jnp.moveaxis(query_rows, 1, 0), jnp.moveaxis(window, 1, 0), jnp.moveaxis(gate_values, 1, 0), starts))
    return outputs.transpose(1, 0, 2, 3).reshape(SEQUENCE_COUNT, SEQUENCE_LENGTH, QUERY_HEADS * HEAD_WIDTH)

def slot_numbers(expert_ids, experts):
    onehot = (expert_ids[:, None] == jnp.arange(experts, dtype=jnp.int32)[None, :]).astype(jnp.int32)
    earlier = jnp.cumsum(onehot, axis=0) - onehot
    return lax.optimization_barrier(jnp.sum(earlier * onehot, axis=1)).astype(jnp.int32)

def expert_layer(moe_input, routes, drop_mask, route_weights, w_gate, w_up, w_down):
    blocks_all = SEQUENCE_COUNT * (SEQUENCE_LENGTH // LOCAL_TOKENS)
    per_block = LOCAL_TOKENS * TOP
    flat_routes = routes.reshape(blocks_all, per_block).astype(jnp.int32)
    slots = jax.vmap(lambda ids: slot_numbers(ids, EXPERTS))(flat_routes)
    sources = jnp.broadcast_to(jnp.arange(blocks_all, dtype=jnp.int32)[:, None], (blocks_all, per_block))
    tokens = sources * LOCAL_TOKENS + (jnp.arange(per_block, dtype=jnp.int32) // TOP)[None, :]
    keep_flags = drop_mask.reshape(blocks_all, per_block)
    weights = keep_flags.astype(jnp.float32) * route_weights.reshape(blocks_all, per_block)
    table_tok = jnp.zeros((EXPERTS, blocks_all, CAP), jnp.int32).at[flat_routes, sources, slots].set(tokens)
    table_keep = jnp.zeros((EXPERTS, blocks_all, CAP), jnp.int32).at[flat_routes, sources, slots].set(keep_flags)
    table_weight = jnp.zeros((EXPERTS, blocks_all, CAP), jnp.float32).at[flat_routes, sources, slots].set(weights)
    tokens_flat = moe_input.reshape(-1, D)

    def per_expert(total, pieces):
        tok_ids, keep_ids, weight_ids, gate_w, up_w, down_w = pieces
        flat_ids = tok_ids.reshape(-1)
        rows = tokens_flat[flat_ids] * keep_ids.reshape(-1, 1).astype(jnp.bfloat16)
        gate_part = jnp.dot(rows.astype(jnp.float32), gate_w.astype(jnp.float32), preferred_element_type=jnp.float32)
        up_part = jnp.dot(rows.astype(jnp.float32), up_w.astype(jnp.float32), preferred_element_type=jnp.float32)
        hidden = (jax.nn.silu(gate_part) * up_part).astype(jnp.bfloat16)
        result = jnp.dot(hidden.astype(jnp.float32), down_w.astype(jnp.float32), preferred_element_type=jnp.float32).astype(jnp.bfloat16)
        total = total.at[flat_ids].add(weight_ids.reshape(-1, 1) * result.astype(jnp.float32))
        return (total, None)
    start = jnp.zeros((blocks_all * LOCAL_TOKENS, D), jnp.float32)
    total, unused = lax.scan(per_expert, start, (table_tok, table_keep, table_weight, w_gate, w_up, w_down))
    return total.astype(jnp.bfloat16).reshape(SEQUENCE_COUNT, SEQUENCE_LENGTH, D)

def reference(delta_query, delta_key, delta_value, delta_gate, delta_beta, delta_decay, norm_gain, attention_query, attention_key_value, attention_gate, moe_input, routes, drop_mask, route_weights, w_gate, w_up, w_down):
    delta_out = delta_layer(delta_query, delta_key, delta_value, delta_gate, delta_beta, delta_decay, norm_gain)
    attn_out = attention_layer(attention_query, attention_key_value, attention_gate)
    moe_out = expert_layer(moe_input, routes, drop_mask, route_weights, w_gate, w_up, w_down)
    return (delta_out, attn_out, moe_out)
```

```python
import math

import jax
import jax.numpy as jnp
from jax import lax
from jax.sharding import PartitionSpec as P

HV = 32
HKD = 16
DK = 128
DV = 128
QUERY_HEADS = 16
KEY_VALUE_HEADS = 2
HEAD_WIDTH = 256
SPAN = 64


precise = lax.Precision.HIGHEST


def carried_state(a, b, axis):
    length, index = (lax.axis_size(axis), lax.axis_index(axis))
    distance = 1
    while distance < length:
        route = [(i, i + distance) for i in range(length - distance)]
        reached = index >= distance
        if 2 * distance >= length:
            b_before = lax.ppermute(b, axis, route)
            b = jnp.einsum("hvk,hkl->hvl", b_before, a, precision=precise) + b
        else:
            a_before, b_before = lax.ppermute((a, b), axis, route)
            joined_a = jnp.einsum("hij,hjk->hik", a_before, a, precision=precise)
            joined_b = jnp.einsum("hvk,hkl->hvl", b_before, a, precision=precise) + b
            a = jnp.where(reached, joined_a, a)
            b = jnp.where(reached, joined_b, b)
        distance *= 2
    return lax.ppermute(b, axis, [(i, i + 1) for i in range(length - 1)])


def shifted(block, axis, distance):
    devices = range(lax.axis_size(axis))
    route = [(i - distance, i) for i in devices if i - distance in devices]
    return lax.ppermute(block, axis, route)


def unit_rows(matrix):
    return matrix / jnp.sqrt(jnp.sum(matrix * matrix, axis=-1, keepdims=True) + 1e-06)


def span_terms(query_rows, keys, value_rows, beta, decay):
    size = decay.shape[-1]
    key_dim = keys.shape[-1]
    value_dim = value_rows.shape[-1]
    cumulative = jnp.cumsum(decay, axis=-1)
    place_list = jnp.arange(size)
    lower = place_list[:, None] >= place_list[None, :]
    strict = place_list[:, None] > place_list[None, :]
    spread = cumulative[..., :, None] - cumulative[..., None, :]
    decay_ratio = jnp.exp(jnp.where(lower, spread, -1e30))
    key_key = jnp.einsum("...ik,...jk->...ij", keys, keys, precision=precise)
    query_key = jnp.einsum("...ik,...jk->...ij", query_rows, keys, precision=precise)
    system = jnp.eye(size, dtype=jnp.float32) + jnp.where(
        strict, beta[..., :, None] * decay_ratio * key_key, 0.0
    )
    retained = jnp.exp(cumulative)
    right_side = jnp.concatenate(
        [beta[..., None] * value_rows, (beta * retained)[..., None] * keys], axis=-1
    )
    solved = jax.scipy.linalg.solve_triangular(system, right_side, lower=True, unit_diagonal=True)
    new_values = solved[..., :value_dim]
    new_keys = solved[..., value_dim:]
    mixing = decay_ratio * query_key
    query_eff = retained[..., None] * query_rows - jnp.einsum(
        "...ij,...jk->...ik", mixing, new_keys, precision=precise
    )
    direct = jnp.einsum("...ij,...jv->...iv", mixing, new_values, precision=precise)
    tail_keys = jnp.exp(cumulative[..., -1:] - cumulative)[..., None] * keys
    carry_a = retained[..., -1:, None] * jnp.eye(key_dim, dtype=jnp.float32) - jnp.einsum(
        "...ck,...cl->...kl", new_keys, tail_keys, precision=precise
    )
    carry_b = jnp.einsum("...cv,...cl->...vl", new_values, tail_keys, precision=precise)
    return (query_eff, direct, carry_a, carry_b)


def gated_norm(outputs, delta_gate, norm_gain):
    scale = lax.rsqrt(jnp.mean(outputs * outputs, axis=-1, keepdims=True) + 1e-06)
    gate_vals = delta_gate.astype(jnp.float32).reshape(outputs.shape)
    normed = outputs * scale * norm_gain * jax.nn.silu(gate_vals)
    return normed.astype(jnp.bfloat16).reshape(delta_gate.shape)


def delta_mixer(
    delta_query, delta_key, delta_value, delta_gate, delta_beta, delta_decay, norm_gain
):
    token_count = delta_query.shape[1]
    n_spans = token_count // SPAN
    head_repeat = HV // HKD
    query_rows = unit_rows(delta_query[0].astype(jnp.float32).reshape(token_count, HKD, DK)) * (
        1.0 / math.sqrt(DK)
    )
    query_rows = jnp.repeat(query_rows, head_repeat, axis=1)
    keys = jnp.repeat(
        unit_rows(delta_key[0].astype(jnp.float32).reshape(token_count, HKD, DK)),
        head_repeat,
        axis=1,
    )
    value_rows = delta_value[0].astype(jnp.float32).reshape(token_count, HV, DV)

    def to_spans(array):
        return array.reshape(n_spans, SPAN, HV, array.shape[-1]).transpose(2, 0, 1, 3)

    query_eff, direct, carry_a, carry_b = span_terms(
        to_spans(query_rows),
        to_spans(keys),
        to_spans(value_rows),
        delta_beta[0].reshape(HV, n_spans, SPAN),
        delta_decay[0].reshape(HV, n_spans, SPAN),
    )
    identity = jnp.broadcast_to(jnp.eye(DK, dtype=jnp.float32), (HV, DK, DK))
    zero_state = jnp.zeros((HV, DV, DK), jnp.float32)
    starts_a = [identity]
    starts_b = [zero_state]
    for span_id in range(n_spans):
        starts_a.append(
            jnp.einsum("hij,hjk->hik", starts_a[-1], carry_a[:, span_id], precision=precise)
        )
        starts_b.append(
            jnp.einsum("hvk,hkl->hvl", starts_b[-1], carry_a[:, span_id], precision=precise)
            + carry_b[:, span_id]
        )
    state_in = carried_state(starts_a[-1], starts_b[-1], "ctx")
    before_a = jnp.stack(starts_a[:-1], axis=1)
    before_b = jnp.stack(starts_b[:-1], axis=1)
    states = jnp.einsum("hvk,hckl->hcvl", state_in, before_a, precision=precise) + before_b
    outputs = jnp.einsum("hcik,hcvk->hciv", query_eff, states, precision=precise) + direct
    outputs = outputs.transpose(1, 2, 0, 3).reshape(token_count, HV, DV)
    return gated_norm(outputs, delta_gate, norm_gain)


def window_attention(attention_query, window_key_value, attention_gate, base):
    local_sequences = attention_query.shape[0]
    token_count = attention_query.shape[1]
    head_groups = QUERY_HEADS // KEY_VALUE_HEADS
    query_rows = attention_query.reshape(
        local_sequences, token_count, KEY_VALUE_HEADS, head_groups, HEAD_WIDTH
    )
    key_value = window_key_value.reshape(
        local_sequences, 2 * token_count, 2, KEY_VALUE_HEADS, HEAD_WIDTH
    )
    scores = jnp.einsum(
        "stkgd,sukd->skgtu", query_rows, key_value[:, :, 0], preferred_element_type=jnp.float32
    ) * (1.0 / math.sqrt(HEAD_WIDTH))
    query_pos = base + jnp.arange(token_count, dtype=jnp.int32)
    key_pos = base - token_count + jnp.arange(2 * token_count, dtype=jnp.int32)
    visible = (
        (key_pos[None, :] <= query_pos[:, None])
        & (key_pos[None, :] > query_pos[:, None] - token_count)
        & (key_pos[None, :] >= 0)
    )
    scores = jnp.where(visible, scores, -jnp.inf)
    row_max = jnp.max(scores, axis=-1, keepdims=True)
    lifted = jnp.exp(scores - row_max)
    probs = (lifted / jnp.sum(lifted, axis=-1, keepdims=True)).astype(jnp.bfloat16)
    mixed = jnp.einsum(
        "skgtu,sukd->stkgd", probs, key_value[:, :, 1], preferred_element_type=jnp.float32
    )
    gated = mixed * jax.nn.sigmoid(attention_gate.astype(jnp.float32).reshape(mixed.shape))
    return gated.astype(jnp.bfloat16).reshape(attention_query.shape)


def slot_numbers(expert_ids, experts):
    row_count = expert_ids.shape[0]
    onehot = (expert_ids[:, None] == jnp.arange(experts, dtype=jnp.int32)[None, :]).astype(
        jnp.bfloat16
    )
    place_list = jnp.arange(row_count, dtype=jnp.int32)
    before = (place_list[:, None] > place_list[None, :]).astype(jnp.bfloat16)
    earlier = jnp.dot(before, onehot, preferred_element_type=jnp.float32)
    return jnp.sum(earlier * onehot.astype(jnp.float32), axis=1).astype(jnp.int32)


def expert_layer(moe_input, routes, drop_mask, route_weights, w_gate, w_up, w_down):
    token_count = moe_input.shape[1]
    width = moe_input.shape[2]
    top_count = routes.shape[2]
    n_seq = lax.axis_size("seq")
    n_ctx = lax.axis_size("ctx")
    n_dev = n_seq * n_ctx
    capacity = max(2, token_count * top_count * 8 // (n_dev * 5))
    expert_ids = routes[0].reshape(-1)
    keep_flags = drop_mask[0].reshape(-1)
    target = expert_ids * capacity + slot_numbers(expert_ids, n_dev)
    rows = jnp.repeat(moe_input[0], top_count, axis=0) * keep_flags[:, None].astype(jnp.bfloat16)
    outgoing = jnp.zeros((n_dev * capacity, width), jnp.bfloat16).at[target].set(rows)
    arrived = lax.all_to_all(
        outgoing.reshape(n_dev, capacity, width),
        ("seq", "ctx"),
        split_axis=0,
        concat_axis=0,
        tiled=True,
    )
    flat_rows = arrived.reshape(-1, width)
    gate_part = jnp.dot(flat_rows, w_gate[0], preferred_element_type=jnp.float32)
    up_part = jnp.dot(flat_rows, w_up[0], preferred_element_type=jnp.float32)
    hidden = (jax.nn.silu(gate_part) * up_part).astype(jnp.bfloat16)
    result = jnp.dot(hidden, w_down[0], preferred_element_type=jnp.float32).astype(jnp.bfloat16)
    returned = lax.all_to_all(
        result.reshape(arrived.shape), ("seq", "ctx"), split_axis=0, concat_axis=0, tiled=True
    )
    results = returned.reshape(n_dev * capacity, width)[target]
    weights = keep_flags.astype(jnp.float32) * route_weights[0].reshape(-1)
    combined = jnp.einsum(
        "tkd,tk->td",
        results.reshape(token_count, top_count, width).astype(jnp.float32),
        weights.reshape(token_count, top_count),
    )
    return combined.astype(jnp.bfloat16)[None]


def body(
    delta_query,
    delta_key,
    delta_value,
    delta_gate,
    delta_beta,
    delta_decay,
    norm_gain,
    attention_query,
    attention_key_value,
    attention_gate,
    moe_input,
    routes,
    drop_mask,
    route_weights,
    w_gate,
    w_up,
    w_down,
):
    delta_out = delta_mixer(
        delta_query, delta_key, delta_value, delta_gate, delta_beta, delta_decay, norm_gain
    )
    previous = shifted(attention_key_value, "ctx", 1)
    window_key_value = jnp.concatenate([previous, attention_key_value], axis=1)
    base = lax.axis_index("ctx") * attention_query.shape[1]
    attn_out = window_attention(attention_query, window_key_value, attention_gate, base)
    moe_out = expert_layer(moe_input, routes, drop_mask, route_weights, w_gate, w_up, w_down)
    return (delta_out, attn_out, moe_out)


def solution(mesh):
    placed = (
        P("seq", "ctx", None),
        P("seq", "ctx", None),
        P("seq", "ctx", None),
        P("seq", "ctx", None),
        P("seq", None, "ctx"),
        P("seq", None, "ctx"),
        P(),
        P("seq", "ctx", None),
        P("seq", "ctx", None),
        P("seq", "ctx", None),
        P("seq", "ctx", None),
        P("seq", "ctx", None),
        P("seq", "ctx", None),
        P("seq", "ctx", None),
        P(("seq", "ctx"), None, None),
        P(("seq", "ctx"), None, None),
        P(("seq", "ctx"), None, None),
    )
    return jax.shard_map(
        body,
        mesh=mesh,
        in_specs=placed,
        out_specs=(P("seq", "ctx", None), P("seq", "ctx", None), P("seq", "ctx", None)),
        check_vma=False,
    )
```

```python
import math

import jax
import jax.numpy as jnp
from jax import lax
from jax.sharding import PartitionSpec as P

HV = 32
HKD = 16
DK = 128
DV = 128
QUERY_HEADS = 16
KEY_VALUE_HEADS = 2
HEAD_WIDTH = 256
SPAN = 32


precise = lax.Precision.HIGHEST


def shifted(block, axis, distance):
    devices = range(lax.axis_size(axis))
    route = [(i - distance, i) for i in devices if i - distance in devices]
    return lax.ppermute(block, axis, route)


def unit_rows(matrix):
    return matrix / jnp.sqrt(jnp.sum(matrix * matrix, axis=-1, keepdims=True) + 1e-06)


def span_terms(query_rows, keys, value_rows, beta, decay):
    size = decay.shape[-1]
    key_dim = keys.shape[-1]
    value_dim = value_rows.shape[-1]
    cumulative = jnp.cumsum(decay, axis=-1)
    place_list = jnp.arange(size)
    lower = place_list[:, None] >= place_list[None, :]
    strict = place_list[:, None] > place_list[None, :]
    spread = cumulative[..., :, None] - cumulative[..., None, :]
    decay_ratio = jnp.exp(jnp.where(lower, spread, -1e30))
    key_key = jnp.einsum("...ik,...jk->...ij", keys, keys, precision=precise)
    query_key = jnp.einsum("...ik,...jk->...ij", query_rows, keys, precision=precise)
    system = jnp.eye(size, dtype=jnp.float32) + jnp.where(
        strict, beta[..., :, None] * decay_ratio * key_key, 0.0
    )
    retained = jnp.exp(cumulative)
    right_side = jnp.concatenate(
        [beta[..., None] * value_rows, (beta * retained)[..., None] * keys], axis=-1
    )
    solved = jax.scipy.linalg.solve_triangular(system, right_side, lower=True, unit_diagonal=True)
    new_values = solved[..., :value_dim]
    new_keys = solved[..., value_dim:]
    mixing = decay_ratio * query_key
    query_eff = retained[..., None] * query_rows - jnp.einsum(
        "...ij,...jk->...ik", mixing, new_keys, precision=precise
    )
    direct = jnp.einsum("...ij,...jv->...iv", mixing, new_values, precision=precise)
    tail_keys = jnp.exp(cumulative[..., -1:] - cumulative)[..., None] * keys
    carry_a = retained[..., -1:, None] * jnp.eye(key_dim, dtype=jnp.float32) - jnp.einsum(
        "...ck,...cl->...kl", new_keys, tail_keys, precision=precise
    )
    carry_b = jnp.einsum("...cv,...cl->...vl", new_values, tail_keys, precision=precise)
    return (query_eff, direct, carry_a, carry_b)


def gated_norm(outputs, delta_gate, norm_gain):
    scale = lax.rsqrt(jnp.mean(outputs * outputs, axis=-1, keepdims=True) + 1e-06)
    gate_vals = delta_gate.astype(jnp.float32).reshape(outputs.shape)
    normed = outputs * scale * norm_gain * jax.nn.silu(gate_vals)
    return normed.astype(jnp.bfloat16).reshape(delta_gate.shape)


def span_prefix(a, b):
    count = a.shape[1]
    eye = jnp.broadcast_to(jnp.eye(a.shape[-1], dtype=a.dtype), a.shape)
    distance = 1
    while distance < count:
        a_before = jnp.concatenate([eye[:, :distance], a[:, : count - distance]], axis=1)
        b_before = jnp.concatenate([jnp.zeros_like(b[:, :distance]), b[:, : count - distance]], axis=1)
        b = jnp.einsum("hcvk,hckl->hcvl", b_before, a, precision=precise) + b
        if 2 * distance < count:
            a = jnp.einsum("hcij,hcjk->hcik", a_before, a, precision=precise)
        distance *= 2
    return jnp.concatenate([jnp.zeros_like(b[:, :1]), b[:, : count - 1]], axis=1)


def delta_mixer(
    delta_query, delta_key, delta_value, delta_gate, delta_beta, delta_decay, norm_gain
):
    token_count = delta_query.shape[1]
    head_repeat = HV // HKD
    heads_here = HV // lax.axis_size("ctx")
    query_raw = jnp.repeat(delta_query[0].reshape(token_count, HKD, DK), head_repeat, axis=1)
    key_raw = jnp.repeat(delta_key[0].reshape(token_count, HKD, DK), head_repeat, axis=1)
    value_raw = delta_value[0].reshape(token_count, HV, DV)
    joined = jnp.concatenate([query_raw, key_raw, value_raw], axis=-1)
    joined = lax.all_to_all(joined, "ctx", split_axis=1, concat_axis=0, tiled=True)
    rates = jnp.stack([delta_beta[0], delta_decay[0]], axis=0)
    rates = lax.all_to_all(rates, "ctx", split_axis=1, concat_axis=2, tiled=True)
    length = joined.shape[0]
    n_spans = length // SPAN
    joined = joined.astype(jnp.float32)
    query_rows = unit_rows(joined[..., :DK]) * (1.0 / math.sqrt(DK))
    keys = unit_rows(joined[..., DK : 2 * DK])
    value_rows = joined[..., 2 * DK :]

    def to_spans(array):
        return array.reshape(n_spans, SPAN, heads_here, array.shape[-1]).transpose(2, 0, 1, 3)

    query_eff, direct, carry_a, carry_b = span_terms(
        to_spans(query_rows),
        to_spans(keys),
        to_spans(value_rows),
        rates[0].reshape(heads_here, n_spans, SPAN),
        rates[1].reshape(heads_here, n_spans, SPAN),
    )
    states = span_prefix(carry_a, carry_b)
    outputs = jnp.einsum("hcik,hcvk->hciv", query_eff, states, precision=precise) + direct
    outputs = outputs.transpose(1, 2, 0, 3).reshape(length, heads_here, DV)
    outputs = lax.all_to_all(outputs, "ctx", split_axis=0, concat_axis=1, tiled=True)
    return gated_norm(outputs, delta_gate, norm_gain)


def window_attention(attention_query, window_key_value, attention_gate, base):
    local_sequences = attention_query.shape[0]
    token_count = attention_query.shape[1]
    head_groups = QUERY_HEADS // KEY_VALUE_HEADS
    query_rows = attention_query.reshape(
        local_sequences, token_count, KEY_VALUE_HEADS, head_groups, HEAD_WIDTH
    )
    key_value = window_key_value.reshape(
        local_sequences, 2 * token_count, 2, KEY_VALUE_HEADS, HEAD_WIDTH
    )
    scores = jnp.einsum(
        "stkgd,sukd->skgtu", query_rows, key_value[:, :, 0], preferred_element_type=jnp.float32
    ) * (1.0 / math.sqrt(HEAD_WIDTH))
    query_pos = base + jnp.arange(token_count, dtype=jnp.int32)
    key_pos = base - token_count + jnp.arange(2 * token_count, dtype=jnp.int32)
    visible = (
        (key_pos[None, :] <= query_pos[:, None])
        & (key_pos[None, :] > query_pos[:, None] - token_count)
        & (key_pos[None, :] >= 0)
    )
    scores = jnp.where(visible, scores, -jnp.inf)
    row_max = jnp.max(scores, axis=-1, keepdims=True)
    lifted = jnp.exp(scores - row_max)
    probs = (lifted / jnp.sum(lifted, axis=-1, keepdims=True)).astype(jnp.bfloat16)
    mixed = jnp.einsum(
        "skgtu,sukd->stkgd", probs, key_value[:, :, 1], preferred_element_type=jnp.float32
    )
    gated = mixed * jax.nn.sigmoid(attention_gate.astype(jnp.float32).reshape(mixed.shape))
    return gated.astype(jnp.bfloat16).reshape(attention_query.shape)


def slot_numbers(expert_ids, experts):
    row_count = expert_ids.shape[0]
    onehot = (expert_ids[:, None] == jnp.arange(experts, dtype=jnp.int32)[None, :]).astype(
        jnp.bfloat16
    )
    place_list = jnp.arange(row_count, dtype=jnp.int32)
    before = (place_list[:, None] > place_list[None, :]).astype(jnp.bfloat16)
    earlier = jnp.dot(before, onehot, preferred_element_type=jnp.float32)
    return jnp.sum(earlier * onehot.astype(jnp.float32), axis=1).astype(jnp.int32)


def expert_layer(moe_input, routes, drop_mask, route_weights, w_gate, w_up, w_down):
    token_count = moe_input.shape[1]
    width = moe_input.shape[2]
    top_count = routes.shape[2]
    n_seq = lax.axis_size("seq")
    n_ctx = lax.axis_size("ctx")
    n_dev = n_seq * n_ctx
    capacity = max(2, token_count * top_count * 8 // (n_dev * 5))
    expert_ids = routes[0].reshape(-1)
    keep_flags = drop_mask[0].reshape(-1)
    target = expert_ids * capacity + slot_numbers(expert_ids, n_dev)
    rows = jnp.repeat(moe_input[0], top_count, axis=0) * keep_flags[:, None].astype(jnp.bfloat16)
    outgoing = jnp.zeros((n_dev * capacity, width), jnp.bfloat16).at[target].set(rows)
    arrived = lax.all_to_all(
        outgoing.reshape(n_dev, capacity, width),
        ("seq", "ctx"),
        split_axis=0,
        concat_axis=0,
        tiled=True,
    )
    flat_rows = arrived.reshape(-1, width)
    gate_part = jnp.dot(flat_rows, w_gate[0], preferred_element_type=jnp.float32)
    up_part = jnp.dot(flat_rows, w_up[0], preferred_element_type=jnp.float32)
    hidden = (jax.nn.silu(gate_part) * up_part).astype(jnp.bfloat16)
    result = jnp.dot(hidden, w_down[0], preferred_element_type=jnp.float32).astype(jnp.bfloat16)
    returned = lax.all_to_all(
        result.reshape(arrived.shape), ("seq", "ctx"), split_axis=0, concat_axis=0, tiled=True
    )
    results = returned.reshape(n_dev * capacity, width)[target]
    weights = keep_flags.astype(jnp.float32) * route_weights[0].reshape(-1)
    combined = jnp.einsum(
        "tkd,tk->td",
        results.reshape(token_count, top_count, width).astype(jnp.float32),
        weights.reshape(token_count, top_count),
    )
    return combined.astype(jnp.bfloat16)[None]


def body(
    delta_query,
    delta_key,
    delta_value,
    delta_gate,
    delta_beta,
    delta_decay,
    norm_gain,
    attention_query,
    attention_key_value,
    attention_gate,
    moe_input,
    routes,
    drop_mask,
    route_weights,
    w_gate,
    w_up,
    w_down,
):
    delta_out = delta_mixer(
        delta_query, delta_key, delta_value, delta_gate, delta_beta, delta_decay, norm_gain
    )
    previous = shifted(attention_key_value, "ctx", 1)
    window_key_value = jnp.concatenate([previous, attention_key_value], axis=1)
    base = lax.axis_index("ctx") * attention_query.shape[1]
    attn_out = window_attention(attention_query, window_key_value, attention_gate, base)
    moe_out = expert_layer(moe_input, routes, drop_mask, route_weights, w_gate, w_up, w_down)
    return (delta_out, attn_out, moe_out)


def solution(mesh):
    placed = (
        P("seq", "ctx", None),
        P("seq", "ctx", None),
        P("seq", "ctx", None),
        P("seq", "ctx", None),
        P("seq", None, "ctx"),
        P("seq", None, "ctx"),
        P(),
        P("seq", "ctx", None),
        P("seq", "ctx", None),
        P("seq", "ctx", None),
        P("seq", "ctx", None),
        P("seq", "ctx", None),
        P("seq", "ctx", None),
        P("seq", "ctx", None),
        P(("seq", "ctx"), None, None),
        P(("seq", "ctx"), None, None),
        P(("seq", "ctx"), None, None),
    )
    return jax.shard_map(
        body,
        mesh=mesh,
        in_specs=placed,
        out_specs=(P("seq", "ctx", None), P("seq", "ctx", None), P("seq", "ctx", None)),
        check_vma=False,
    )
```

```python
import math

import jax
import jax.numpy as jnp
from jax import lax
from jax.sharding import PartitionSpec as P

HV = 32
HKD = 16
DK = 128
DV = 128
QUERY_HEADS = 16
KEY_VALUE_HEADS = 2
HEAD_WIDTH = 256
SPAN = 32


precise = lax.Precision.HIGHEST


def shifted(block, axis, distance):
    devices = range(lax.axis_size(axis))
    route = [(i - distance, i) for i in devices if i - distance in devices]
    return lax.ppermute(block, axis, route)


def unit_rows(matrix):
    return matrix / jnp.sqrt(jnp.sum(matrix * matrix, axis=-1, keepdims=True) + 1e-06)


def span_terms(query_rows, keys, value_rows, beta, decay):
    size = decay.shape[-1]
    key_dim = keys.shape[-1]
    value_dim = value_rows.shape[-1]
    cumulative = jnp.cumsum(decay, axis=-1)
    place_list = jnp.arange(size)
    lower = place_list[:, None] >= place_list[None, :]
    strict = place_list[:, None] > place_list[None, :]
    spread = cumulative[..., :, None] - cumulative[..., None, :]
    decay_ratio = jnp.exp(jnp.where(lower, spread, -1e30))
    key_key = jnp.einsum("...ik,...jk->...ij", keys, keys, precision=precise)
    query_key = jnp.einsum("...ik,...jk->...ij", query_rows, keys, precision=precise)
    system = jnp.eye(size, dtype=jnp.float32) + jnp.where(
        strict, beta[..., :, None] * decay_ratio * key_key, 0.0
    )
    retained = jnp.exp(cumulative)
    right_side = jnp.concatenate(
        [beta[..., None] * value_rows, (beta * retained)[..., None] * keys], axis=-1
    )
    solved = jax.scipy.linalg.solve_triangular(system, right_side, lower=True, unit_diagonal=True)
    new_values = solved[..., :value_dim]
    new_keys = solved[..., value_dim:]
    mixing = decay_ratio * query_key
    query_eff = retained[..., None] * query_rows - jnp.einsum(
        "...ij,...jk->...ik", mixing, new_keys, precision=precise
    )
    direct = jnp.einsum("...ij,...jv->...iv", mixing, new_values, precision=precise)
    tail_keys = jnp.exp(cumulative[..., -1:] - cumulative)[..., None] * keys
    carry_a = retained[..., -1:, None] * jnp.eye(key_dim, dtype=jnp.float32) - jnp.einsum(
        "...ck,...cl->...kl", new_keys, tail_keys, precision=precise
    )
    carry_b = jnp.einsum("...cv,...cl->...vl", new_values, tail_keys, precision=precise)
    return (query_eff, direct, carry_a, carry_b)


def gated_norm(outputs, delta_gate, norm_gain):
    scale = lax.rsqrt(jnp.mean(outputs * outputs, axis=-1, keepdims=True) + 1e-06)
    gate_vals = delta_gate.astype(jnp.float32).reshape(outputs.shape)
    normed = outputs * scale * norm_gain * jax.nn.silu(gate_vals)
    return normed.astype(jnp.bfloat16).reshape(delta_gate.shape)


def span_prefix(a, b):
    count = a.shape[1]
    if count == 1:
        return jnp.zeros_like(b)
    a_even, a_odd = a[:, 0::2], a[:, 1::2]
    b_even, b_odd = b[:, 0::2], b[:, 1::2]
    pair_b = jnp.einsum("hcvk,hckl->hcvl", b_even, a_odd, precision=precise) + b_odd
    if count > 2:
        pair_a = jnp.einsum("hcij,hcjk->hcik", a_even, a_odd, precision=precise)
    else:
        pair_a = a_odd
    before_even = span_prefix(pair_a, pair_b)
    before_odd = jnp.einsum("hcvk,hckl->hcvl", before_even, a_even, precision=precise) + b_even
    joined = jnp.stack([before_even, before_odd], axis=2)
    return joined.reshape(b.shape)


def delta_mixer(
    delta_query, delta_key, delta_value, delta_gate, delta_beta, delta_decay, norm_gain
):
    token_count = delta_query.shape[1]
    head_repeat = HV // HKD
    heads_here = HV // lax.axis_size("ctx")
    query_raw = jnp.repeat(delta_query[0].reshape(token_count, HKD, DK), head_repeat, axis=1)
    key_raw = jnp.repeat(delta_key[0].reshape(token_count, HKD, DK), head_repeat, axis=1)
    value_raw = delta_value[0].reshape(token_count, HV, DV)
    joined = jnp.concatenate([query_raw, key_raw, value_raw], axis=-1)
    joined = lax.all_to_all(joined, "ctx", split_axis=1, concat_axis=0, tiled=True)
    rates = jnp.stack([delta_beta[0], delta_decay[0]], axis=0)
    rates = lax.all_to_all(rates, "ctx", split_axis=1, concat_axis=2, tiled=True)
    length = joined.shape[0]
    n_spans = length // SPAN
    joined = joined.astype(jnp.float32)
    query_rows = unit_rows(joined[..., :DK]) * (1.0 / math.sqrt(DK))
    keys = unit_rows(joined[..., DK : 2 * DK])
    value_rows = joined[..., 2 * DK :]

    def to_spans(array):
        return array.reshape(n_spans, SPAN, heads_here, array.shape[-1]).transpose(2, 0, 1, 3)

    query_eff, direct, carry_a, carry_b = span_terms(
        to_spans(query_rows),
        to_spans(keys),
        to_spans(value_rows),
        rates[0].reshape(heads_here, n_spans, SPAN),
        rates[1].reshape(heads_here, n_spans, SPAN),
    )
    states = span_prefix(carry_a, carry_b)
    outputs = jnp.einsum("hcik,hcvk->hciv", query_eff, states, precision=precise) + direct
    outputs = outputs.transpose(1, 2, 0, 3).reshape(length, heads_here, DV)
    outputs = lax.all_to_all(outputs, "ctx", split_axis=0, concat_axis=1, tiled=True)
    return gated_norm(outputs, delta_gate, norm_gain)


def window_attention(attention_query, window_key_value, attention_gate, base):
    local_sequences = attention_query.shape[0]
    token_count = attention_query.shape[1]
    head_groups = QUERY_HEADS // KEY_VALUE_HEADS
    query_rows = attention_query.reshape(
        local_sequences, token_count, KEY_VALUE_HEADS, head_groups, HEAD_WIDTH
    )
    key_value = window_key_value.reshape(
        local_sequences, 2 * token_count, 2, KEY_VALUE_HEADS, HEAD_WIDTH
    )
    scores = jnp.einsum(
        "stkgd,sukd->skgtu", query_rows, key_value[:, :, 0], preferred_element_type=jnp.float32
    ) * (1.0 / math.sqrt(HEAD_WIDTH))
    query_pos = base + jnp.arange(token_count, dtype=jnp.int32)
    key_pos = base - token_count + jnp.arange(2 * token_count, dtype=jnp.int32)
    visible = (
        (key_pos[None, :] <= query_pos[:, None])
        & (key_pos[None, :] > query_pos[:, None] - token_count)
        & (key_pos[None, :] >= 0)
    )
    scores = jnp.where(visible, scores, -jnp.inf)
    row_max = jnp.max(scores, axis=-1, keepdims=True)
    lifted = jnp.exp(scores - row_max)
    probs = (lifted / jnp.sum(lifted, axis=-1, keepdims=True)).astype(jnp.bfloat16)
    mixed = jnp.einsum(
        "skgtu,sukd->stkgd", probs, key_value[:, :, 1], preferred_element_type=jnp.float32
    )
    gated = mixed * jax.nn.sigmoid(attention_gate.astype(jnp.float32).reshape(mixed.shape))
    return gated.astype(jnp.bfloat16).reshape(attention_query.shape)


def slot_numbers(expert_ids, experts):
    row_count = expert_ids.shape[0]
    onehot = (expert_ids[:, None] == jnp.arange(experts, dtype=jnp.int32)[None, :]).astype(
        jnp.bfloat16
    )
    place_list = jnp.arange(row_count, dtype=jnp.int32)
    before = (place_list[:, None] > place_list[None, :]).astype(jnp.bfloat16)
    earlier = jnp.dot(before, onehot, preferred_element_type=jnp.float32)
    return jnp.sum(earlier * onehot.astype(jnp.float32), axis=1).astype(jnp.int32)


def expert_layer(moe_input, routes, drop_mask, route_weights, w_gate, w_up, w_down):
    token_count = moe_input.shape[1]
    width = moe_input.shape[2]
    top_count = routes.shape[2]
    n_seq = lax.axis_size("seq")
    n_ctx = lax.axis_size("ctx")
    n_dev = n_seq * n_ctx
    capacity = max(2, token_count * top_count * 8 // (n_dev * 5))
    expert_ids = routes[0].reshape(-1)
    keep_flags = drop_mask[0].reshape(-1)
    target = expert_ids * capacity + slot_numbers(expert_ids, n_dev)
    rows = jnp.repeat(moe_input[0], top_count, axis=0) * keep_flags[:, None].astype(jnp.bfloat16)
    outgoing = jnp.zeros((n_dev * capacity, width), jnp.bfloat16).at[target].set(rows)
    arrived = lax.all_to_all(
        outgoing.reshape(n_dev, capacity, width),
        ("seq", "ctx"),
        split_axis=0,
        concat_axis=0,
        tiled=True,
    )
    flat_rows = arrived.reshape(-1, width)
    gate_part = jnp.dot(flat_rows, w_gate[0], preferred_element_type=jnp.float32)
    up_part = jnp.dot(flat_rows, w_up[0], preferred_element_type=jnp.float32)
    hidden = (jax.nn.silu(gate_part) * up_part).astype(jnp.bfloat16)
    result = jnp.dot(hidden, w_down[0], preferred_element_type=jnp.float32).astype(jnp.bfloat16)
    returned = lax.all_to_all(
        result.reshape(arrived.shape), ("seq", "ctx"), split_axis=0, concat_axis=0, tiled=True
    )
    results = returned.reshape(n_dev * capacity, width)[target]
    weights = keep_flags.astype(jnp.float32) * route_weights[0].reshape(-1)
    combined = jnp.einsum(
        "tkd,tk->td",
        results.reshape(token_count, top_count, width).astype(jnp.float32),
        weights.reshape(token_count, top_count),
    )
    return combined.astype(jnp.bfloat16)[None]


def body(
    delta_query,
    delta_key,
    delta_value,
    delta_gate,
    delta_beta,
    delta_decay,
    norm_gain,
    attention_query,
    attention_key_value,
    attention_gate,
    moe_input,
    routes,
    drop_mask,
    route_weights,
    w_gate,
    w_up,
    w_down,
):
    delta_out = delta_mixer(
        delta_query, delta_key, delta_value, delta_gate, delta_beta, delta_decay, norm_gain
    )
    previous = shifted(attention_key_value, "ctx", 1)
    window_key_value = jnp.concatenate([previous, attention_key_value], axis=1)
    base = lax.axis_index("ctx") * attention_query.shape[1]
    attn_out = window_attention(attention_query, window_key_value, attention_gate, base)
    moe_out = expert_layer(moe_input, routes, drop_mask, route_weights, w_gate, w_up, w_down)
    return (delta_out, attn_out, moe_out)


def solution(mesh):
    placed = (
        P("seq", "ctx", None),
        P("seq", "ctx", None),
        P("seq", "ctx", None),
        P("seq", "ctx", None),
        P("seq", None, "ctx"),
        P("seq", None, "ctx"),
        P(),
        P("seq", "ctx", None),
        P("seq", "ctx", None),
        P("seq", "ctx", None),
        P("seq", "ctx", None),
        P("seq", "ctx", None),
        P("seq", "ctx", None),
        P("seq", "ctx", None),
        P(("seq", "ctx"), None, None),
        P(("seq", "ctx"), None, None),
        P(("seq", "ctx"), None, None),
    )
    return jax.shard_map(
        body,
        mesh=mesh,
        in_specs=placed,
        out_specs=(P("seq", "ctx", None), P("seq", "ctx", None), P("seq", "ctx", None)),
        check_vma=False,
    )
```

```python
import math

import jax
import jax.numpy as jnp
from jax import lax
from jax.sharding import PartitionSpec as P

HV = 32
HKD = 16
DK = 128
DV = 128
QUERY_HEADS = 16
KEY_VALUE_HEADS = 2
HEAD_WIDTH = 256
SPAN = 16


precise = lax.Precision.HIGHEST


def shifted(block, axis, distance):
    devices = range(lax.axis_size(axis))
    route = [(i - distance, i) for i in devices if i - distance in devices]
    return lax.ppermute(block, axis, route)


def unit_rows(matrix):
    return matrix / jnp.sqrt(jnp.sum(matrix * matrix, axis=-1, keepdims=True) + 1e-06)


def span_terms(query_rows, keys, value_rows, beta, decay):
    size = decay.shape[-1]
    key_dim = keys.shape[-1]
    value_dim = value_rows.shape[-1]
    cumulative = jnp.cumsum(decay, axis=-1)
    place_list = jnp.arange(size)
    lower = place_list[:, None] >= place_list[None, :]
    strict = place_list[:, None] > place_list[None, :]
    spread = cumulative[..., :, None] - cumulative[..., None, :]
    decay_ratio = jnp.exp(jnp.where(lower, spread, -1e30))
    key_key = jnp.einsum("...ik,...jk->...ij", keys, keys, precision=precise)
    query_key = jnp.einsum("...ik,...jk->...ij", query_rows, keys, precision=precise)
    system = jnp.eye(size, dtype=jnp.float32) + jnp.where(
        strict, beta[..., :, None] * decay_ratio * key_key, 0.0
    )
    retained = jnp.exp(cumulative)
    right_side = jnp.concatenate(
        [beta[..., None] * value_rows, (beta * retained)[..., None] * keys], axis=-1
    )
    solved = jax.scipy.linalg.solve_triangular(system, right_side, lower=True, unit_diagonal=True)
    new_values = solved[..., :value_dim]
    new_keys = solved[..., value_dim:]
    mixing = decay_ratio * query_key
    query_eff = retained[..., None] * query_rows - jnp.einsum(
        "...ij,...jk->...ik", mixing, new_keys, precision=precise
    )
    direct = jnp.einsum("...ij,...jv->...iv", mixing, new_values, precision=precise)
    tail_keys = jnp.exp(cumulative[..., -1:] - cumulative)[..., None] * keys
    carry_a = retained[..., -1:, None] * jnp.eye(key_dim, dtype=jnp.float32) - jnp.einsum(
        "...ck,...cl->...kl", new_keys, tail_keys, precision=precise
    )
    carry_b = jnp.einsum("...cv,...cl->...vl", new_values, tail_keys, precision=precise)
    return (query_eff, direct, carry_a, carry_b)


def gated_norm(outputs, delta_gate, norm_gain):
    scale = lax.rsqrt(jnp.mean(outputs * outputs, axis=-1, keepdims=True) + 1e-06)
    gate_vals = delta_gate.astype(jnp.float32).reshape(outputs.shape)
    normed = outputs * scale * norm_gain * jax.nn.silu(gate_vals)
    return normed.astype(jnp.bfloat16).reshape(delta_gate.shape)


def span_prefix(a, b):
    count = a.shape[1]
    if count == 1:
        return jnp.zeros_like(b)
    a_even, a_odd = a[:, 0::2], a[:, 1::2]
    b_even, b_odd = b[:, 0::2], b[:, 1::2]
    pair_b = jnp.einsum("hcvk,hckl->hcvl", b_even, a_odd, precision=precise) + b_odd
    if count > 2:
        pair_a = jnp.einsum("hcij,hcjk->hcik", a_even, a_odd, precision=precise)
    else:
        pair_a = a_odd
    before_even = span_prefix(pair_a, pair_b)
    before_odd = jnp.einsum("hcvk,hckl->hcvl", before_even, a_even, precision=precise) + b_even
    joined = jnp.stack([before_even, before_odd], axis=2)
    return joined.reshape(b.shape)


def delta_mixer(
    delta_query, delta_key, delta_value, delta_gate, delta_beta, delta_decay, norm_gain
):
    token_count = delta_query.shape[1]
    head_repeat = HV // HKD
    heads_here = HV // lax.axis_size("ctx")
    query_raw = jnp.repeat(delta_query[0].reshape(token_count, HKD, DK), head_repeat, axis=1)
    key_raw = jnp.repeat(delta_key[0].reshape(token_count, HKD, DK), head_repeat, axis=1)
    value_raw = delta_value[0].reshape(token_count, HV, DV)
    joined = jnp.concatenate([query_raw, key_raw, value_raw], axis=-1)
    joined = lax.all_to_all(joined, "ctx", split_axis=1, concat_axis=0, tiled=True)
    rates = jnp.stack([delta_beta[0], delta_decay[0]], axis=0)
    rates = lax.all_to_all(rates, "ctx", split_axis=1, concat_axis=2, tiled=True)
    length = joined.shape[0]
    n_spans = length // SPAN
    joined = joined.astype(jnp.float32)
    query_rows = unit_rows(joined[..., :DK]) * (1.0 / math.sqrt(DK))
    keys = unit_rows(joined[..., DK : 2 * DK])
    value_rows = joined[..., 2 * DK :]

    def to_spans(array):
        return array.reshape(n_spans, SPAN, heads_here, array.shape[-1]).transpose(2, 0, 1, 3)

    query_eff, direct, carry_a, carry_b = span_terms(
        to_spans(query_rows),
        to_spans(keys),
        to_spans(value_rows),
        rates[0].reshape(heads_here, n_spans, SPAN),
        rates[1].reshape(heads_here, n_spans, SPAN),
    )
    states = span_prefix(carry_a, carry_b)
    outputs = jnp.einsum("hcik,hcvk->hciv", query_eff, states, precision=precise) + direct
    outputs = outputs.transpose(1, 2, 0, 3).reshape(length, heads_here, DV)
    outputs = lax.all_to_all(outputs, "ctx", split_axis=0, concat_axis=1, tiled=True)
    return gated_norm(outputs, delta_gate, norm_gain)


def window_attention(attention_query, window_key_value, attention_gate, base):
    local_sequences = attention_query.shape[0]
    token_count = attention_query.shape[1]
    head_groups = QUERY_HEADS // KEY_VALUE_HEADS
    query_rows = attention_query.reshape(
        local_sequences, token_count, KEY_VALUE_HEADS, head_groups, HEAD_WIDTH
    )
    key_value = window_key_value.reshape(
        local_sequences, 2 * token_count, 2, KEY_VALUE_HEADS, HEAD_WIDTH
    )
    scores = jnp.einsum(
        "stkgd,sukd->skgtu", query_rows, key_value[:, :, 0], preferred_element_type=jnp.float32
    ) * (1.0 / math.sqrt(HEAD_WIDTH))
    query_pos = base + jnp.arange(token_count, dtype=jnp.int32)
    key_pos = base - token_count + jnp.arange(2 * token_count, dtype=jnp.int32)
    visible = (
        (key_pos[None, :] <= query_pos[:, None])
        & (key_pos[None, :] > query_pos[:, None] - token_count)
        & (key_pos[None, :] >= 0)
    )
    scores = jnp.where(visible, scores, -jnp.inf)
    row_max = jnp.max(scores, axis=-1, keepdims=True)
    lifted = jnp.exp(scores - row_max)
    probs = (lifted / jnp.sum(lifted, axis=-1, keepdims=True)).astype(jnp.bfloat16)
    mixed = jnp.einsum(
        "skgtu,sukd->stkgd", probs, key_value[:, :, 1], preferred_element_type=jnp.float32
    )
    gated = mixed * jax.nn.sigmoid(attention_gate.astype(jnp.float32).reshape(mixed.shape))
    return gated.astype(jnp.bfloat16).reshape(attention_query.shape)


def slot_numbers(expert_ids, experts):
    row_count = expert_ids.shape[0]
    onehot = (expert_ids[:, None] == jnp.arange(experts, dtype=jnp.int32)[None, :]).astype(
        jnp.bfloat16
    )
    place_list = jnp.arange(row_count, dtype=jnp.int32)
    before = (place_list[:, None] > place_list[None, :]).astype(jnp.bfloat16)
    earlier = jnp.dot(before, onehot, preferred_element_type=jnp.float32)
    return jnp.sum(earlier * onehot.astype(jnp.float32), axis=1).astype(jnp.int32)


def expert_layer(moe_input, routes, drop_mask, route_weights, w_gate, w_up, w_down):
    token_count = moe_input.shape[1]
    width = moe_input.shape[2]
    top_count = routes.shape[2]
    n_seq = lax.axis_size("seq")
    n_ctx = lax.axis_size("ctx")
    n_dev = n_seq * n_ctx
    capacity = max(2, token_count * top_count * 8 // (n_dev * 5))
    expert_ids = routes[0].reshape(-1)
    keep_flags = drop_mask[0].reshape(-1)
    target = expert_ids * capacity + slot_numbers(expert_ids, n_dev)
    rows = jnp.repeat(moe_input[0], top_count, axis=0) * keep_flags[:, None].astype(jnp.bfloat16)
    outgoing = jnp.zeros((n_dev * capacity, width), jnp.bfloat16).at[target].set(rows)
    arrived = lax.all_to_all(
        outgoing.reshape(n_dev, capacity, width),
        ("seq", "ctx"),
        split_axis=0,
        concat_axis=0,
        tiled=True,
    )
    flat_rows = arrived.reshape(-1, width)
    gate_part = jnp.dot(flat_rows, w_gate[0], preferred_element_type=jnp.float32)
    up_part = jnp.dot(flat_rows, w_up[0], preferred_element_type=jnp.float32)
    hidden = (jax.nn.silu(gate_part) * up_part).astype(jnp.bfloat16)
    result = jnp.dot(hidden, w_down[0], preferred_element_type=jnp.float32).astype(jnp.bfloat16)
    returned = lax.all_to_all(
        result.reshape(arrived.shape), ("seq", "ctx"), split_axis=0, concat_axis=0, tiled=True
    )
    results = returned.reshape(n_dev * capacity, width)[target]
    weights = keep_flags.astype(jnp.float32) * route_weights[0].reshape(-1)
    combined = jnp.einsum(
        "tkd,tk->td",
        results.reshape(token_count, top_count, width).astype(jnp.float32),
        weights.reshape(token_count, top_count),
    )
    return combined.astype(jnp.bfloat16)[None]


def body(
    delta_query,
    delta_key,
    delta_value,
    delta_gate,
    delta_beta,
    delta_decay,
    norm_gain,
    attention_query,
    attention_key_value,
    attention_gate,
    moe_input,
    routes,
    drop_mask,
    route_weights,
    w_gate,
    w_up,
    w_down,
):
    delta_out = delta_mixer(
        delta_query, delta_key, delta_value, delta_gate, delta_beta, delta_decay, norm_gain
    )
    previous = shifted(attention_key_value, "ctx", 1)
    window_key_value = jnp.concatenate([previous, attention_key_value], axis=1)
    base = lax.axis_index("ctx") * attention_query.shape[1]
    attn_out = window_attention(attention_query, window_key_value, attention_gate, base)
    moe_out = expert_layer(moe_input, routes, drop_mask, route_weights, w_gate, w_up, w_down)
    return (delta_out, attn_out, moe_out)


def solution(mesh):
    placed = (
        P("seq", "ctx", None),
        P("seq", "ctx", None),
        P("seq", "ctx", None),
        P("seq", "ctx", None),
        P("seq", None, "ctx"),
        P("seq", None, "ctx"),
        P(),
        P("seq", "ctx", None),
        P("seq", "ctx", None),
        P("seq", "ctx", None),
        P("seq", "ctx", None),
        P("seq", "ctx", None),
        P("seq", "ctx", None),
        P("seq", "ctx", None),
        P(("seq", "ctx"), None, None),
        P(("seq", "ctx"), None, None),
        P(("seq", "ctx"), None, None),
    )
    return jax.shard_map(
        body,
        mesh=mesh,
        in_specs=placed,
        out_specs=(P("seq", "ctx", None), P("seq", "ctx", None), P("seq", "ctx", None)),
        check_vma=False,
    )
```
